512 devices in a mesh: seq: 32 (over x, y, core), mp: 16 (over z).
Axes of the slice: x: 4, y: 4, z: 16, core: 2. Of those that a mesh axis runs over, the one named last changes fastest.
Arguments:
- token_ids: int32 [256, 4], replicated, may hold values from 0 to 151935
- embedding: bfloat16 [151936, 1536], P('seq', 'mp'), may hold values from -13 to 13
- attn_gain: float32 [1536], P('mp'), may hold values from 0.25 to 1.75
- w_qkv: bfloat16 [1536, 2048], P('mp', 'seq'), may hold values from -0.15625 to 0.15625
- w_out: bfloat16 [1536, 1536], P('seq', 'mp'), may hold values from -0.15625 to 0.15625
- prompt_cache: bfloat16 [2, 32, 2048, 256], P(None, 'mp', 'seq'), may hold values from -170 to 170
- request_cache: bfloat16 [2, 256, 2048, 256], P(None, 'mp', 'seq'), may hold values from -170 to 170
- group_ids: int32 [256], P('mp'), may hold values from 0 to 1
- prefix_len: int32 [32], P('mp'), may hold values from 1 to 2048
- suffix_len: int32 [256], P('mp'), may hold values from 0 to 2048
- moe_gain: float32 [1536], replicated, may hold values from 0.25 to 1.75
- w_router: bfloat16 [1536, 32], replicated, may hold values from -0.15625 to 0.15625
- w_gate_up: bfloat16 [32, 2, 768, 1536], P('seq', None, 'mp'), may hold values from -0.15625 to 0.15625
- w_down: bfloat16 [32, 768, 1536], P('seq', 'mp'), may hold values from -0.21875 to 0.21875
- routes: int32 [256, 4, 4], replicated, may hold values from 0 to 31, all different within a row; in each aligned block of 32 rows (0 to 31, 32 to 63, ..., all dimensions but the last counted through in order) at most 8 rows name the same one
Outputs:
- hidden_out: bfloat16 [256, 4, 1536], P('seq', None, 'mp')
The draws below stay inside these ranges and needn't reach their ends.
Inputs may be any that keep to these rules, and one draw needn't show every extreme that they name: `routes`: in each aligned block of 32 rows (request, step) taken in order, the requests of one index of seq, no expert is named more than 8 times.
All inputs are finite; a program needn't handle non-finite values.
Results may differ from the reference program's by a relative error of at most 0.015.
The reference program's roundings to bfloat16 on the way count: a program that leaves them out, or rounds other values in their place, can miss the bound.
Values may be sent and summed in bfloat16 or wider, within the bound.
No kernel may reach another device: no remote copies, remote signals or barrier semaphores. Data moves between devices by JAX's collectives and lax.ppermute only.
A program may use at most 128 MiB of HBM per device.

```python
import math
import jax
import jax.numpy as jnp
import numpy as np
from jax import lax

D = 1536
QUERY_HEADS = 12
KEY_VALUE_HEADS = 2
HEAD_SIZE = 128
E = 32
FF = 768
TOPK = 4
VOCAB = 151936
NEW_TOKENS = 4
REQ_DEV = 16
PRE_DEV = 64
SUF_DEV = 64
R = 256
TOK_SEQ = 8
G_DEV = 2
G = 32
PMAX = 2048
SMAX = 2048
QUERY_FEATURES = 1536
KEY_FEATURES = 256
QKVW = 2048
MOST = 8
CAP = 256
N_SEQ = 32


def cache_pair(key, shape):
    key_keys, key_vals = jax.random.split(key, 2)
    stored_keys = 2.0 * jax.random.truncated_normal(key_keys, -4.0, 4.0, shape)
    values = jax.random.truncated_normal(key_vals, -4.0, 4.0, shape)
    return jnp.stack([stored_keys, values]).astype(jnp.bfloat16)


def draw_prompt_cache(key, part):
    return cache_pair(jax.random.fold_in(key, 11), (G, PMAX, KEY_FEATURES))


def draw_request_cache(key, part):
    return cache_pair(jax.random.fold_in(key, 12), (R, SMAX, KEY_FEATURES))


def draw_embedding(key, part):
    key_base, key_rows, key_cols = jax.random.split(jax.random.fold_in(key, 13), 3)
    row_scale = jnp.exp(jax.random.uniform(key_rows, (VOCAB, 1), minval=-1.15, maxval=1.15))
    col_scale = jnp.exp(jax.random.uniform(key_cols, (1, D), minval=-1.15, maxval=1.15))
    base_draw = jax.random.truncated_normal(key_base, -4.0, 4.0, (VOCAB, D))
    return (0.3 * base_draw * row_scale * col_scale).astype(jnp.bfloat16)


def touch_ends(entries, own_key, least, top_value):
    longest = entries.shape.index(max(entries.shape))
    spots = []
    for shift in (0, 1):
        where = [jax.random.randint(jax.random.fold_in(own_key, axis), (), 0, length) for axis, length in enumerate(entries.shape)]
        where[longest] = (where[longest] + shift) % entries.shape[longest]
        spots.append(tuple(where))
    return entries.at[spots[0]].set(least).at[spots[1]].set(top_value)


def level_of(rng, dims, shards, smallest, top_value):
    def one(position, shards_of):
        draws = jax.random.uniform(jax.random.fold_in(jax.random.fold_in(rng, 6), position), (shards_of,), jnp.float32, smallest / len(shards), top_value / len(shards))
        return jnp.repeat(jnp.exp(draws), dims[position] // shards_of).reshape((-1,) + (1,) * (len(dims) - position - 1))

    level = one(*shards[0])
    for cut in shards[1:]:
        level = level * one(*cut)
    return level


def ranked_wide(rng, extent, number_of, lean):
    weights = [min(1 << octave, number_of + 1 - (1 << octave)) * (1 << 20) // math.isqrt((1 << octave) ** lean) + 1 for octave in range((number_of + 1).bit_length()) if 1 << octave <= number_of]
    width = 1 + sum(weights) // (1 << 30)
    table = np.cumsum(np.array([max(1, weight // width) for weight in weights]))
    pick = jax.random.randint(jax.random.fold_in(rng, 1), extent, 0, int(table[len(weights) - 1]))
    start = jnp.left_shift(1, jnp.searchsorted(jnp.asarray(table, jnp.int32), pick, side="right").astype(jnp.int32))
    standing = start - 1 + jax.random.randint(jax.random.fold_in(rng, 4), extent, 0, 1 << 30) % jnp.minimum(start, number_of + 1 - start)
    return jax.random.permutation(jax.random.fold_in(rng, 2), number_of)[standing].astype(jnp.int32)


def assign_block(key, own, number, rows, count, top, most, slope):
    sequence = jax.random.permutation(key, count)
    heavy_load, usual = load_shares(count, rows * top, most, slope, True), load_shares(count, rows * top, most, slope, False)
    places = jnp.arange(count)

    def named(tallies, rotation):
        used = int((tallies > 0).sum())
        fixed = max(1, used // 4)
        passed = fixed + (places - fixed + rotation * (used - fixed)) % max(1, count - fixed)
        return jnp.zeros((count,), jnp.int32).at[sequence[jnp.where(places < fixed, places, passed)]].set(jnp.asarray(tallies, jnp.int32))

    tallies = jnp.where(number % 4 == 0, named(heavy_load, number // 4), named(usual, number - number // 4 - 1))
    mixed = jax.random.permutation(jax.random.fold_in(own, 3), count)
    source_of, sink = mixed[0:count // 2 * 2:2], mixed[1:count // 2 * 2:2]
    margin = jnp.minimum(tallies[source_of] - 1, most - tallies[sink]) // 2
    margin = jnp.where((source_of == sequence[0]) | (sink == sequence[0]) | (tallies[sink] == 0), 0, jnp.maximum(margin, 0))
    passed = jax.random.randint(jax.random.fold_in(own, 4), (count // 2,), 0, 1 << 20) % (margin + 1)
    tallies = tallies.at[source_of].add(-passed).at[sink].add(passed)
    members = jnp.searchsorted(jnp.cumsum(tallies), jnp.arange(rows * top), side="right").astype(jnp.int32)
    grid = members.reshape(top, rows).T
    grid = grid[jax.random.permutation(jax.random.fold_in(own, 1), rows)]
    rotation = jax.random.randint(jax.random.fold_in(own, 2), (rows, 1), 0, top)
    return jnp.take_along_axis(grid, (jnp.arange(top)[None, :] + rotation) % top, axis=1)


def load_shares(amount, total, reach, lean, full):
    loads = [(1 << 20) // math.isqrt(grade ** lean) + 1 for grade in range(1, amount + 1)]
    largest = reach if full else min(reach, max(-(-total // amount), total * loads[0] // sum(loads)))
    least = 1 if total - largest >= amount - 1 else 0
    counts, spare = [largest] + [least] * (amount - 1), total - largest - least * (amount - 1)
    while spare > 0:
        free = [i for i in range(1, amount) if counts[i] < largest] or [i for i in range(1, amount) if counts[i] < reach]
        mass, left = sum([loads[i] for i in free]), spare
        for i in free:
            addition = min(reach - counts[i], max(1, left * loads[i] // mass), spare)
            counts[i] = counts[i] + addition
            spare = spare - addition
    return np.array(counts)


def bell_draw(rng, dims, deviation, bound, shards=(), kind=jnp.bfloat16):
    drawn = jax.random.normal(rng, dims, jnp.float32) * deviation
    if len(shards) > 0:
        drawn = level_of(rng, dims, shards, -0.22, 0.18) * drawn
    return jnp.clip(drawn, min=-bound, max=bound).astype(kind)


def setup_inputs(seed: int = 0) -> dict:
    seeds = jax.random.split(jax.random.key(seed), 16)
    token_ids = touch_ends(ranked_wide(seeds[0], (R, NEW_TOKENS), VOCAB, 2), jax.random.fold_in(seeds[0], 3), 0, VOCAB - 1).astype(jnp.int32)
    embedding = draw_embedding(jax.random.fold_in(seeds[15], 71), 0)
    attn_gain = jnp.clip(1.0 + 0.15 * jax.random.normal(seeds[2], (D,), jnp.float32), 0.25, 1.75)
    w_qkv = bell_draw(seeds[3], (D, QKVW), D ** -0.5, 0.15625, ((0, 16), (1, 32)))
    w_out = bell_draw(seeds[4], (QUERY_FEATURES, D), QUERY_FEATURES ** -0.5, 0.15625, ((0, 32), (1, 16)))
    prompt_cache = draw_prompt_cache(jax.random.fold_in(seeds[15], 71), 0)
    request_cache = draw_request_cache(jax.random.fold_in(seeds[15], 71), 0)
    group_ids = touch_ends(jax.random.randint(seeds[7], (R,), 0, G_DEV), jax.random.fold_in(seeds[7], 1), 0, G_DEV - 1).astype(jnp.int32)
    prefix_len = touch_ends(jax.random.randint(seeds[8], (G,), 1, PMAX + 1), jax.random.fold_in(seeds[8], 1), 1, PMAX).astype(jnp.int32)
    suffix_len = touch_ends(jax.random.randint(seeds[9], (R,), 0, SMAX + 1), jax.random.fold_in(seeds[9], 1), 0, SMAX).astype(jnp.int32)
    moe_gain = jnp.clip(1.0 + 0.15 * jax.random.normal(seeds[10], (D,), jnp.float32), 0.25, 1.75)
    w_router = bell_draw(seeds[11], (D, E), D ** -0.5, 0.15625)
    w_gate_up = bell_draw(seeds[12], (E, 2, FF, D), D ** -0.5, 0.15625, ((0, 32), (2, 16)))
    w_down = bell_draw(seeds[13], (E, FF, D), FF ** -0.5, 0.21875, ((0, 32), (1, 16)))
    routes_keys = jax.random.split(jax.random.fold_in(seeds[14], 1), R * NEW_TOKENS // (TOK_SEQ * NEW_TOKENS))
    routes_turns = jax.random.permutation(jax.random.fold_in(seeds[14], 3), R * NEW_TOKENS // (TOK_SEQ * NEW_TOKENS))
    routes = jax.vmap(lambda own, number: assign_block(jax.random.fold_in(seeds[14], 2), own, number, TOK_SEQ * NEW_TOKENS, E, TOPK, MOST, 2))(routes_keys, routes_turns).reshape((R, NEW_TOKENS, TOPK))
    return dict(token_ids=token_ids, embedding=embedding, attn_gain=attn_gain, w_qkv=w_qkv, w_out=w_out, prompt_cache=prompt_cache, request_cache=request_cache, group_ids=group_ids, prefix_len=prefix_len, suffix_len=suffix_len, moe_gain=moe_gain, w_router=w_router, w_gate_up=w_gate_up, w_down=w_down, routes=routes)


EPS = 1e-06
NEG = -1e+30

def rounded_float(values):
    return lax.optimization_barrier(values.astype(jnp.bfloat16)).astype(jnp.float32)

def norm_rows(values, gain_vec):
    floats = values.astype(jnp.float32)
    mean_sq = lax.optimization_barrier(jnp.mean(floats * floats, axis=-1, keepdims=True))
    return (floats * lax.rsqrt(mean_sq + EPS) * gain_vec).astype(jnp.bfloat16)

def reference(token_ids, embedding, attn_gain, w_qkv, w_out, prompt_cache, request_cache, group_ids, prefix_len, suffix_len, moe_gain, w_router, w_gate_up, w_down, routes):
    resid = embedding[token_ids]
    normed = norm_rows(resid, attn_gain)
    projected_rows = jnp.dot(normed.reshape(R * NEW_TOKENS, D), w_qkv, preferred_element_type=jnp.float32)
    projected_rows = projected_rows.astype(jnp.bfloat16).reshape(R, NEW_TOKENS, QKVW)
    owners = jnp.arange(R, dtype=jnp.int32) // REQ_DEV * G_DEV + group_ids
    score_scale = 1.0 / math.sqrt(HEAD_SIZE)
    requests_per_group = QUERY_HEADS // KEY_VALUE_HEADS
    block_span_width = PRE_DEV + SUF_DEV

    def attend_one(inputs):
        query_row_list, request = inputs
        owner = owners[request]
        query_matrix = query_row_list[:, :QUERY_FEATURES].astype(jnp.float32).reshape(NEW_TOKENS, KEY_VALUE_HEADS, requests_per_group, HEAD_SIZE)
        fresh_key_rows = query_row_list[:, QUERY_FEATURES:QUERY_FEATURES + KEY_FEATURES].astype(jnp.float32).reshape(NEW_TOKENS, KEY_VALUE_HEADS, HEAD_SIZE)
        fresh_value_rows = query_row_list[:, QUERY_FEATURES + KEY_FEATURES:].astype(jnp.float32).reshape(NEW_TOKENS, KEY_VALUE_HEADS, HEAD_SIZE)
        key_block_list = jnp.concatenate([prompt_cache[0, owner].reshape(N_SEQ, PRE_DEV, KEY_FEATURES), request_cache[0, request].reshape(N_SEQ, SUF_DEV, KEY_FEATURES)], axis=1)
        value_blocks = jnp.concatenate([prompt_cache[1, owner].reshape(N_SEQ, PRE_DEV, KEY_FEATURES), request_cache[1, request].reshape(N_SEQ, SUF_DEV, KEY_FEATURES)], axis=1)
        key_block_list = key_block_list.astype(jnp.float32).reshape(N_SEQ, block_span_width, KEY_VALUE_HEADS, HEAD_SIZE)
        value_blocks = value_blocks.astype(jnp.float32).reshape(N_SEQ, block_span_width, KEY_VALUE_HEADS, HEAD_SIZE)
        pre_pos = jnp.arange(N_SEQ, dtype=jnp.int32)[:, None] * PRE_DEV + jnp.arange(PRE_DEV, dtype=jnp.int32)[None, :]
        suf_pos = jnp.arange(N_SEQ, dtype=jnp.int32)[:, None] * SUF_DEV + jnp.arange(SUF_DEV, dtype=jnp.int32)[None, :]
        valid_pos = jnp.concatenate([pre_pos < prefix_len[owner], suf_pos < suffix_len[request]], axis=1)
        valid_mask = valid_pos[:, None, None, None, :]
        scores = jnp.einsum('tkgd,blkd->btkgl', query_matrix, key_block_list) * score_scale
        scores = jnp.where(valid_mask, scores, NEG)
        block_max = lax.optimization_barrier(jnp.max(scores, axis=-1))
        block_probs = jnp.where(valid_mask, jnp.exp(scores - block_max[..., None]), 0.0)
        block_sum = lax.optimization_barrier(jnp.sum(block_probs, axis=-1))
        block_acc = jnp.einsum('btkgl,blkd->btkgd', rounded_float(block_probs), value_blocks)
        new_scores = jnp.einsum('tkgd,ukd->tkgu', query_matrix, fresh_key_rows) * score_scale
        causal = (jnp.arange(NEW_TOKENS)[:, None] >= jnp.arange(NEW_TOKENS)[None, :])[:, None, None, :]
        new_scores = jnp.where(causal, new_scores, NEG)
        new_max = lax.optimization_barrier(jnp.max(new_scores, axis=-1))
        new_probs = jnp.where(causal, jnp.exp(new_scores - new_max[..., None]), 0.0)
        new_sum = lax.optimization_barrier(jnp.sum(new_probs, axis=-1))
        new_acc = jnp.einsum('tkgu,ukd->tkgd', rounded_float(new_probs), fresh_value_rows)
        overall = jnp.maximum(lax.optimization_barrier(jnp.max(block_max, axis=0)), new_max)
        block_weight = jnp.exp(block_max - overall)
        new_weight = jnp.exp(new_max - overall)
        denominator = lax.optimization_barrier(jnp.sum(block_weight * block_sum, axis=0)) + new_weight * new_sum
        weighted = lax.optimization_barrier(jnp.sum(block_weight[..., None] * block_acc, axis=0)) + new_weight[..., None] * new_acc
        return (weighted / denominator[..., None]).reshape(NEW_TOKENS, QUERY_FEATURES).astype(jnp.bfloat16)
    attended = lax.map(attend_one, (projected_rows, jnp.arange(R, dtype=jnp.int32)))
    out_rows = jnp.dot(attended.reshape(R * NEW_TOKENS, QUERY_FEATURES), w_out, preferred_element_type=jnp.float32)
    resid = (resid.astype(jnp.float32) + out_rows.reshape(R, NEW_TOKENS, D)).astype(jnp.bfloat16)
    token_rows = resid.reshape(R * NEW_TOKENS, D)
    normed_moe = norm_rows(token_rows, moe_gain)
    logits = jnp.dot(normed_moe, w_router, preferred_element_type=jnp.float32)
    route_rows = routes.reshape(R * NEW_TOKENS, TOPK)
    picked_logits = jnp.take_along_axis(logits, route_rows, axis=1)
    route_weights = jnp.exp(picked_logits) / lax.optimization_barrier(jnp.sum(jnp.exp(picked_logits), axis=1, keepdims=True))

    def expert_step(carry, inputs):
        gate_up, down_proj, expert = inputs
        hit_rows = jnp.any(route_rows == expert, axis=1)
        row_ids = jnp.nonzero(hit_rows, size=CAP, fill_value=0)[0].astype(jnp.int32)
        live_rows = jnp.arange(CAP, dtype=jnp.int32) < jnp.sum(hit_rows.astype(jnp.int32))
        chosen = normed_moe[row_ids]
        both = lax.dot_general(chosen, gate_up.reshape(2 * FF, D), (((1,), (1,)), ((), ())), preferred_element_type=jnp.float32)
        hidden = (jnp.maximum(both[:, :FF], 0.0) * both[:, FF:]).astype(jnp.bfloat16)
        expert_out = jnp.dot(hidden, down_proj, preferred_element_type=jnp.float32).astype(jnp.bfloat16)
        share = lax.optimization_barrier(jnp.sum(jnp.where(route_rows[row_ids] == expert, route_weights[row_ids], 0.0), axis=1))
        term = (share[:, None] * expert_out.astype(jnp.float32)).astype(jnp.bfloat16).astype(jnp.float32)
        term = jnp.where(live_rows[:, None], term, 0.0)
        return (carry.at[row_ids].add(term), None)
    start_sum = jnp.zeros((R * NEW_TOKENS, D), jnp.float32)
    moe_sum, _ = lax.scan(expert_step, start_sum, (w_gate_up, w_down, jnp.arange(E, dtype=jnp.int32)))
    final_rows = (token_rows.astype(jnp.float32) + moe_sum).astype(jnp.bfloat16)
    return final_rows.reshape(R, NEW_TOKENS, D)
```

```python
import math

import numpy as np

import jax
import jax.numpy as jnp
from jax import lax
from jax.sharding import PartitionSpec as P

D = 1536
QUERY_HEADS = 12
KEY_VALUE_HEADS = 2
HEAD_SIZE = 128
E = 32
TOPK = 4
NEW_TOKENS = 4
MOST = 8

EPS = 1e-06
NEG = -1e30


def exchange(values, axis):
    return lax.all_to_all(values, axis, 0, 0, tiled=True)


def on_device(
    token_ids,
    embedding,
    attn_gain,
    w_qkv,
    w_out,
    prompt_cache,
    request_cache,
    group_ids,
    prefix_len,
    suffix_len,
    moe_gain,
    w_router,
    w_gate_up,
    w_down,
    routes,
):
    n_seq = lax.axis_size("seq")
    n_mp = lax.axis_size("mp")
    s = lax.axis_index("seq")
    total_rows = token_ids.shape[0] * NEW_TOKENS
    home_rows = total_rows // n_seq
    feat_mp = embedding.shape[1]

    vocab_rows = embedding.shape[0]
    local_ids = token_ids.reshape(total_rows) - s * vocab_rows
    inside = (local_ids >= 0) & (local_ids < vocab_rows)
    looked = jnp.take(embedding, jnp.clip(local_ids, 0, vocab_rows - 1), axis=0)
    looked = jnp.where(inside[:, None], looked, jnp.zeros_like(looked))
    got = exchange(looked.reshape(n_seq, home_rows, feat_mp), "seq")
    x_home = jnp.sum(got.astype(jnp.float32), axis=0)

    square_sum = lax.psum(jnp.sum(x_home * x_home, axis=-1), "mp")
    normed = (x_home * lax.rsqrt(square_sum[:, None] / D + EPS) * attn_gain).astype(jnp.bfloat16)
    normed_all = lax.all_gather(normed, "seq", axis=0, tiled=True)

    qkv_part = jnp.dot(normed_all, w_qkv, preferred_element_type=jnp.float32)
    attn_rows = total_rows // n_mp
    qkv_got = exchange(qkv_part.reshape(n_mp, attn_rows, qkv_part.shape[-1]), "mp")
    qkv_cols = jnp.sum(qkv_got, axis=0).astype(jnp.bfloat16)
    qkv_rows = lax.all_gather(qkv_cols, "seq", axis=1, tiled=True)

    request_count = group_ids.shape[0]
    groups_per = QUERY_HEADS // KEY_VALUE_HEADS
    qf = QUERY_HEADS * HEAD_SIZE
    kf = KEY_VALUE_HEADS * HEAD_SIZE
    q = qkv_rows[:, :qf].reshape(request_count, NEW_TOKENS, KEY_VALUE_HEADS, groups_per, HEAD_SIZE)
    k_new = qkv_rows[:, qf : qf + kf].reshape(request_count, NEW_TOKENS, KEY_VALUE_HEADS, HEAD_SIZE)
    v_new = qkv_rows[:, qf + kf :].reshape(request_count, NEW_TOKENS, KEY_VALUE_HEADS, HEAD_SIZE)

    pre_rows = prompt_cache.shape[2]
    suf_rows = request_cache.shape[2]
    first_group = (group_ids == 0)[:, None, None]
    pre_k = jnp.where(first_group, prompt_cache[0, 0][None], prompt_cache[0, 1][None])
    pre_v = jnp.where(first_group, prompt_cache[1, 0][None], prompt_cache[1, 1][None])
    keys = jnp.concatenate([pre_k, request_cache[0]], axis=1).reshape(
        request_count, pre_rows + suf_rows, KEY_VALUE_HEADS, HEAD_SIZE
    )
    values = jnp.concatenate([pre_v, request_cache[1]], axis=1).reshape(
        request_count, pre_rows + suf_rows, KEY_VALUE_HEADS, HEAD_SIZE
    )
    own_prefix = jnp.where(group_ids == 0, prefix_len[0], prefix_len[1])
    pre_pos = s * pre_rows + jnp.arange(pre_rows, dtype=jnp.int32)
    suf_pos = s * suf_rows + jnp.arange(suf_rows, dtype=jnp.int32)
    valid = jnp.concatenate(
        [pre_pos[None, :] < own_prefix[:, None], suf_pos[None, :] < suffix_len[:, None]], axis=1
    )[:, None, None, None, :]
    score_scale = 1.0 / math.sqrt(HEAD_SIZE)
    scores = jnp.einsum("jtkgd,jpkd->jtkgp", q, keys, preferred_element_type=jnp.float32) * score_scale
    scores = jnp.where(valid, scores, NEG)
    block_max = jnp.max(scores, axis=-1)
    probs = jnp.where(valid, jnp.exp(scores - block_max[..., None]), 0.0)
    block_sum = jnp.sum(probs, axis=-1)
    block_acc = jnp.einsum(
        "jtkgp,jpkd->jtkgd", probs.astype(jnp.bfloat16), values, preferred_element_type=jnp.float32
    )

    new_scores = jnp.einsum("jtkgd,jukd->jtkgu", q, k_new, preferred_element_type=jnp.float32) * score_scale
    causal = (jnp.arange(NEW_TOKENS)[:, None] >= jnp.arange(NEW_TOKENS)[None, :])[None, :, None, None, :]
    new_scores = jnp.where(causal, new_scores, NEG)
    new_max = jnp.max(new_scores, axis=-1)
    new_probs = jnp.where(causal, jnp.exp(new_scores - new_max[..., None]), 0.0)
    new_sum = jnp.sum(new_probs, axis=-1)
    new_acc = jnp.einsum(
        "jtkgu,jukd->jtkgd", new_probs.astype(jnp.bfloat16), v_new, preferred_element_type=jnp.float32
    )

    fs = qf // n_seq
    acc_flat = block_acc.reshape(attn_rows, qf)
    acc_parts = acc_flat.reshape(attn_rows, n_seq, fs).transpose(1, 0, 2)
    head_pick = np.array([[(i * fs) // HEAD_SIZE, (i * fs + fs - 1) // HEAD_SIZE] for i in range(n_seq)])
    max_flat = block_max.reshape(attn_rows, QUERY_HEADS)
    sum_flat = block_sum.reshape(attn_rows, QUERY_HEADS)
    max_parts = max_flat[:, head_pick].transpose(1, 0, 2)
    sum_parts = sum_flat[:, head_pick].transpose(1, 0, 2)
    merged = exchange(jnp.concatenate([acc_parts, max_parts, sum_parts], axis=-1), "seq")
    got_acc = merged[..., :fs]
    feat_ids = s * fs + jnp.arange(fs, dtype=jnp.int32)
    second = (feat_ids // HEAD_SIZE - (s * fs) // HEAD_SIZE) == 1
    got_max = jnp.where(second, merged[..., fs + 1 : fs + 2], merged[..., fs : fs + 1])
    got_sum = jnp.where(second, merged[..., fs + 3 : fs + 4], merged[..., fs + 2 : fs + 3])
    own_heads = feat_ids // HEAD_SIZE
    n_max = jnp.take(new_max.reshape(attn_rows, QUERY_HEADS), own_heads, axis=1)
    n_sum = jnp.take(new_sum.reshape(attn_rows, QUERY_HEADS), own_heads, axis=1)
    n_acc = lax.dynamic_slice_in_dim(new_acc.reshape(attn_rows, qf), s * fs, fs, 1)
    overall = jnp.maximum(jnp.max(got_max, axis=0), n_max)
    cache_weight = jnp.exp(got_max - overall)
    own_weight = jnp.exp(n_max - overall)
    denominator = jnp.sum(cache_weight * got_sum, axis=0) + own_weight * n_sum
    numerator = jnp.sum(cache_weight * got_acc, axis=0) + own_weight * n_acc
    attended = (numerator / denominator).astype(jnp.bfloat16)

    att_all = lax.all_gather(attended, "mp", axis=0, tiled=True)
    out_part = jnp.dot(att_all, w_out, preferred_element_type=jnp.float32)
    out_got = exchange(out_part.reshape(n_seq, home_rows, out_part.shape[-1]), "seq")
    x2 = (x_home + jnp.sum(out_got, axis=0)).astype(jnp.bfloat16)

    route_blocks = routes.reshape(n_seq, home_rows, TOPK)
    experts_all = jnp.arange(E, dtype=jnp.int32)
    hit = jnp.any(route_blocks[:, :, :, None] == experts_all, axis=2)
    hit_count = hit.astype(jnp.int32)
    ahead = jnp.cumsum(hit_count, axis=1) - hit_count
    chosen = hit[..., None] & (ahead[..., None] == jnp.arange(MOST, dtype=jnp.int32))
    chosen = jnp.transpose(chosen, (0, 2, 3, 1)).astype(jnp.bfloat16)
    member = hit.astype(jnp.bfloat16)

    home_table = chosen[s]
    dispatch = jnp.einsum("esr,rf->esf", home_table, x2, preferred_element_type=jnp.float32).astype(
        jnp.bfloat16
    )
    slot_rows = exchange(dispatch, "seq")
    slot_full = lax.all_gather(slot_rows, "mp", axis=2, tiled=True).reshape(n_seq * MOST, D)

    expert = s
    expert_table = chosen[:, expert]
    slot_member = jnp.einsum(
        "bsr,bre->bse", expert_table, member, preferred_element_type=jnp.float32
    ).reshape(n_seq * MOST, E)
    floats2 = slot_full.astype(jnp.float32)
    mean_sq = jnp.mean(floats2 * floats2, axis=-1, keepdims=True)
    normed2 = (floats2 * lax.rsqrt(mean_sq + EPS) * moe_gain).astype(jnp.bfloat16)
    logits = jnp.dot(normed2, w_router, preferred_element_type=jnp.float32)
    which = (experts_all == expert).astype(jnp.float32)
    own_flag = jnp.sum(slot_member * which, axis=1)
    own_logit = jnp.sum(logits * which, axis=1)
    denom = jnp.sum(jnp.where(slot_member > 0, jnp.exp(logits), 0.0), axis=1)
    share = own_flag * jnp.exp(own_logit) / (denom + 1.0 - own_flag)

    gate_up = w_gate_up[0]
    half = gate_up.shape[1]
    both = lax.dot_general(
        normed2,
        gate_up.reshape(2 * half, D),
        (((1,), (1,)), ((), ())),
        preferred_element_type=jnp.float32,
    )
    hidden = (jnp.maximum(both[:, :half], 0.0) * both[:, half:]).astype(jnp.bfloat16)
    down_part = jnp.dot(hidden, w_down[0], preferred_element_type=jnp.float32).astype(jnp.bfloat16)
    down_got = exchange(
        down_part.reshape(n_seq * MOST, n_mp, feat_mp).transpose(1, 0, 2), "mp"
    )
    expert_out = jnp.sum(down_got.astype(jnp.float32), axis=0).astype(jnp.bfloat16)
    weighted = (share[:, None] * expert_out.astype(jnp.float32)).astype(jnp.bfloat16)
    back = exchange(weighted.reshape(n_seq, MOST, feat_mp), "seq")
    terms = jnp.einsum("esr,esf->rf", home_table, back, preferred_element_type=jnp.float32)
    final = (x2.astype(jnp.float32) + terms).astype(jnp.bfloat16)
    return final.reshape(home_rows // NEW_TOKENS, NEW_TOKENS, feat_mp)


def solution(mesh):
    in_specs = (
        P(),
        P("seq", "mp"),
        P("mp"),
        P("mp", "seq"),
        P("seq", "mp"),
        P(None, "mp", "seq", None),
        P(None, "mp", "seq", None),
        P("mp"),
        P("mp"),
        P("mp"),
        P(),
        P(),
        P("seq", None, "mp", None),
        P("seq", "mp", None),
        P(),
    )
    out_specs = P("seq", None, "mp")
    return jax.shard_map(
        on_device, mesh=mesh, in_specs=in_specs, out_specs=out_specs, check_vma=False
    )
```

```python
import math

import numpy as np

import jax
import jax.numpy as jnp
from jax import lax
from jax.sharding import PartitionSpec as P

D = 1536
QUERY_HEADS = 12
KEY_VALUE_HEADS = 2
HEAD_SIZE = 128
E = 32
TOPK = 4
NEW_TOKENS = 4
MOST = 8

EPS = 1e-06
NEG = -1e30


def exchange(values, axis):
    return lax.all_to_all(values, axis, 0, 0, tiled=True)


def gather_by_exchange(values, axis, n):
    return lax.all_to_all(jnp.broadcast_to(values[None], (n,) + values.shape), axis, 0, 0, tiled=True)


def on_device(
    token_ids,
    embedding,
    attn_gain,
    w_qkv,
    w_out,
    prompt_cache,
    request_cache,
    group_ids,
    prefix_len,
    suffix_len,
    moe_gain,
    w_router,
    w_gate_up,
    w_down,
    routes,
):
    n_seq = lax.axis_size("seq")
    n_mp = lax.axis_size("mp")
    s = lax.axis_index("seq")
    total_rows = token_ids.shape[0] * NEW_TOKENS
    home_rows = total_rows // n_seq
    feat_mp = embedding.shape[1]

    vocab_rows = embedding.shape[0]
    local_ids = token_ids.reshape(total_rows) - s * vocab_rows
    inside = (local_ids >= 0) & (local_ids < vocab_rows)
    looked = jnp.take(embedding, jnp.clip(local_ids, 0, vocab_rows - 1), axis=0)
    looked = jnp.where(inside[:, None], looked, jnp.zeros_like(looked))
    got = exchange(looked.reshape(n_seq, home_rows, feat_mp), "seq")
    x_home = jnp.sum(got.astype(jnp.float32), axis=0)

    square_sum = jnp.sum(gather_by_exchange(jnp.sum(x_home * x_home, axis=-1), "mp", n_mp), axis=0)
    normed = (x_home * lax.rsqrt(square_sum[:, None] / D + EPS) * attn_gain).astype(jnp.bfloat16)
    normed_all = gather_by_exchange(normed, "seq", n_seq).reshape(total_rows, feat_mp)

    qkv_part = jnp.dot(normed_all, w_qkv, preferred_element_type=jnp.float32)
    attn_rows = total_rows // n_mp
    qkv_got = exchange(qkv_part.reshape(n_mp, attn_rows, qkv_part.shape[-1]), "mp")
    qkv_cols = jnp.sum(qkv_got, axis=0).astype(jnp.bfloat16)
    qkv_rows = gather_by_exchange(qkv_cols, "seq", n_seq).transpose(1, 0, 2).reshape(attn_rows, -1)

    request_count = group_ids.shape[0]
    groups_per = QUERY_HEADS // KEY_VALUE_HEADS
    qf = QUERY_HEADS * HEAD_SIZE
    kf = KEY_VALUE_HEADS * HEAD_SIZE
    q = qkv_rows[:, :qf].reshape(request_count, NEW_TOKENS, KEY_VALUE_HEADS, groups_per, HEAD_SIZE)
    k_new = qkv_rows[:, qf : qf + kf].reshape(request_count, NEW_TOKENS, KEY_VALUE_HEADS, HEAD_SIZE)
    v_new = qkv_rows[:, qf + kf :].reshape(request_count, NEW_TOKENS, KEY_VALUE_HEADS, HEAD_SIZE)

    pre_rows = prompt_cache.shape[2]
    suf_rows = request_cache.shape[2]
    first_group = (group_ids == 0)[:, None, None]
    pre_k = jnp.where(first_group, prompt_cache[0, 0][None], prompt_cache[0, 1][None])
    pre_v = jnp.where(first_group, prompt_cache[1, 0][None], prompt_cache[1, 1][None])
    keys = jnp.concatenate([pre_k, request_cache[0]], axis=1).reshape(
        request_count, pre_rows + suf_rows, KEY_VALUE_HEADS, HEAD_SIZE
    )
    values = jnp.concatenate([pre_v, request_cache[1]], axis=1).reshape(
        request_count, pre_rows + suf_rows, KEY_VALUE_HEADS, HEAD_SIZE
    )
    own_prefix = jnp.where(group_ids == 0, prefix_len[0], prefix_len[1])
    pre_pos = s * pre_rows + jnp.arange(pre_rows, dtype=jnp.int32)
    suf_pos = s * suf_rows + jnp.arange(suf_rows, dtype=jnp.int32)
    valid = jnp.concatenate(
        [pre_pos[None, :] < own_prefix[:, None], suf_pos[None, :] < suffix_len[:, None]], axis=1
    )[:, None, None, None, :]
    score_scale = 1.0 / math.sqrt(HEAD_SIZE)
    scores = jnp.einsum("jtkgd,jpkd->jtkgp", q, keys, preferred_element_type=jnp.float32) * score_scale
    scores = jnp.where(valid, scores, NEG)
    block_max = jnp.max(scores, axis=-1)
    probs = jnp.where(valid, jnp.exp(scores - block_max[..., None]), 0.0)
    block_sum = jnp.sum(probs, axis=-1)
    block_acc = jnp.einsum(
        "jtkgp,jpkd->jtkgd", probs.astype(jnp.bfloat16), values, preferred_element_type=jnp.float32
    )

    new_scores = jnp.einsum("jtkgd,jukd->jtkgu", q, k_new, preferred_element_type=jnp.float32) * score_scale
    causal = (jnp.arange(NEW_TOKENS)[:, None] >= jnp.arange(NEW_TOKENS)[None, :])[None, :, None, None, :]
    new_scores = jnp.where(causal, new_scores, NEG)
    new_max = jnp.max(new_scores, axis=-1)
    new_probs = jnp.where(causal, jnp.exp(new_scores - new_max[..., None]), 0.0)
    new_sum = jnp.sum(new_probs, axis=-1)
    new_acc = jnp.einsum(
        "jtkgu,jukd->jtkgd", new_probs.astype(jnp.bfloat16), v_new, preferred_element_type=jnp.float32
    )

    fs = qf // n_seq
    acc_flat = block_acc.reshape(attn_rows, qf)
    acc_parts = acc_flat.reshape(attn_rows, n_seq, fs).transpose(1, 0, 2)
    head_pick = np.array([[(i * fs) // HEAD_SIZE, (i * fs + fs - 1) // HEAD_SIZE] for i in range(n_seq)])
    max_flat = block_max.reshape(attn_rows, QUERY_HEADS)
    sum_flat = block_sum.reshape(attn_rows, QUERY_HEADS)
    max_parts = max_flat[:, head_pick].transpose(1, 0, 2)
    sum_parts = sum_flat[:, head_pick].transpose(1, 0, 2)
    merged = exchange(jnp.concatenate([acc_parts, max_parts, sum_parts], axis=-1), "seq")
    got_acc = merged[..., :fs]
    feat_ids = s * fs + jnp.arange(fs, dtype=jnp.int32)
    second = (feat_ids // HEAD_SIZE - (s * fs) // HEAD_SIZE) == 1
    got_max = jnp.where(second, merged[..., fs + 1 : fs + 2], merged[..., fs : fs + 1])
    got_sum = jnp.where(second, merged[..., fs + 3 : fs + 4], merged[..., fs + 2 : fs + 3])
    own_heads = feat_ids // HEAD_SIZE
    n_max = jnp.take(new_max.reshape(attn_rows, QUERY_HEADS), own_heads, axis=1)
    n_sum = jnp.take(new_sum.reshape(attn_rows, QUERY_HEADS), own_heads, axis=1)
    n_acc = lax.dynamic_slice_in_dim(new_acc.reshape(attn_rows, qf), s * fs, fs, 1)
    overall = jnp.maximum(jnp.max(got_max, axis=0), n_max)
    cache_weight = jnp.exp(got_max - overall)
    own_weight = jnp.exp(n_max - overall)
    denominator = jnp.sum(cache_weight * got_sum, axis=0) + own_weight * n_sum
    numerator = jnp.sum(cache_weight * got_acc, axis=0) + own_weight * n_acc
    attended = (numerator / denominator).astype(jnp.bfloat16)

    att_all = gather_by_exchange(attended, "mp", n_mp).reshape(total_rows, fs)
    out_part = jnp.dot(att_all, w_out, preferred_element_type=jnp.float32)
    out_got = exchange(out_part.reshape(n_seq, home_rows, out_part.shape[-1]), "seq")
    x2 = (x_home + jnp.sum(out_got, axis=0)).astype(jnp.bfloat16)

    route_blocks = routes.reshape(n_seq, home_rows, TOPK)
    experts_all = jnp.arange(E, dtype=jnp.int32)
    hit = jnp.any(route_blocks[:, :, :, None] == experts_all, axis=2)
    hit_count = hit.astype(jnp.int32)
    ahead = jnp.cumsum(hit_count, axis=1) - hit_count
    chosen = hit[..., None] & (ahead[..., None] == jnp.arange(MOST, dtype=jnp.int32))
    chosen = jnp.transpose(chosen, (0, 2, 3, 1)).astype(jnp.bfloat16)
    member = hit.astype(jnp.bfloat16)

    home_table = chosen[s]
    dispatch = jnp.einsum("esr,rf->esf", home_table, x2, preferred_element_type=jnp.float32).astype(
        jnp.bfloat16
    )
    slot_rows = exchange(dispatch, "seq")
    slot_full = gather_by_exchange(slot_rows, "mp", n_mp).transpose(1, 2, 0, 3).reshape(n_seq * MOST, D)

    expert = s
    expert_table = chosen[:, expert]
    slot_member = jnp.einsum(
        "bsr,bre->bse", expert_table, member, preferred_element_type=jnp.float32
    ).reshape(n_seq * MOST, E)
    floats2 = slot_full.astype(jnp.float32)
    mean_sq = jnp.mean(floats2 * floats2, axis=-1, keepdims=True)
    normed2 = (floats2 * lax.rsqrt(mean_sq + EPS) * moe_gain).astype(jnp.bfloat16)
    logits = jnp.dot(normed2, w_router, preferred_element_type=jnp.float32)
    which = (experts_all == expert).astype(jnp.float32)
    own_flag = jnp.sum(slot_member * which, axis=1)
    own_logit = jnp.sum(logits * which, axis=1)
    denom = jnp.sum(jnp.where(slot_member > 0, jnp.exp(logits), 0.0), axis=1)
    share = own_flag * jnp.exp(own_logit) / (denom + 1.0 - own_flag)

    gate_up = w_gate_up[0]
    half = gate_up.shape[1]
    both = lax.dot_general(
        normed2,
        gate_up.reshape(2 * half, D),
        (((1,), (1,)), ((), ())),
        preferred_element_type=jnp.float32,
    )
    hidden = (jnp.maximum(both[:, :half], 0.0) * both[:, half:]).astype(jnp.bfloat16)
    down_part = jnp.dot(hidden, w_down[0], preferred_element_type=jnp.float32).astype(jnp.bfloat16)
    down_got = exchange(
        down_part.reshape(n_seq * MOST, n_mp, feat_mp).transpose(1, 0, 2), "mp"
    )
    expert_out = jnp.sum(down_got.astype(jnp.float32), axis=0).astype(jnp.bfloat16)
    weighted = (share[:, None] * expert_out.astype(jnp.float32)).astype(jnp.bfloat16)
    back = exchange(weighted.reshape(n_seq, MOST, feat_mp), "seq")
    terms = jnp.einsum("esr,esf->rf", home_table, back, preferred_element_type=jnp.float32)
    final = (x2.astype(jnp.float32) + terms).astype(jnp.bfloat16)
    return final.reshape(home_rows // NEW_TOKENS, NEW_TOKENS, feat_mp)


def solution(mesh):
    in_specs = (
        P(),
        P("seq", "mp"),
        P("mp"),
        P("mp", "seq"),
        P("seq", "mp"),
        P(None, "mp", "seq", None),
        P(None, "mp", "seq", None),
        P("mp"),
        P("mp"),
        P("mp"),
        P(),
        P(),
        P("seq", None, "mp", None),
        P("seq", "mp", None),
        P(),
    )
    out_specs = P("seq", None, "mp")
    return jax.shard_map(
        on_device, mesh=mesh, in_specs=in_specs, out_specs=out_specs, check_vma=False
    )
```

```python
import math

import numpy as np

import jax
import jax.numpy as jnp
from jax import lax
from jax.sharding import PartitionSpec as P

D = 1536
QUERY_HEADS = 12
KEY_VALUE_HEADS = 2
HEAD_SIZE = 128
E = 32
TOPK = 4
NEW_TOKENS = 4
MOST = 8

EPS = 1e-06
NEG = -1e30


def exchange(values, axis):
    return lax.all_to_all(values, axis, 0, 0, tiled=True)


def gather_by_exchange(values, axis, n):
    return lax.all_to_all(jnp.broadcast_to(values[None], (n,) + values.shape), axis, 0, 0, tiled=True)


def on_device(
    token_ids,
    embedding,
    attn_gain,
    w_qkv,
    w_out,
    prompt_cache,
    request_cache,
    group_ids,
    prefix_len,
    suffix_len,
    moe_gain,
    w_router,
    w_gate_up,
    w_down,
    routes,
):
    n_seq = lax.axis_size("seq")
    n_mp = lax.axis_size("mp")
    s = lax.axis_index("seq")
    total_rows = token_ids.shape[0] * NEW_TOKENS
    home_rows = total_rows // n_seq
    feat_mp = embedding.shape[1]

    vocab_rows = embedding.shape[0]
    local_ids = token_ids.reshape(total_rows) - s * vocab_rows
    inside = (local_ids >= 0) & (local_ids < vocab_rows)
    looked = jnp.take(embedding, jnp.clip(local_ids, 0, vocab_rows - 1), axis=0)
    looked = jnp.where(inside[:, None], looked, jnp.zeros_like(looked))
    got = exchange(looked.reshape(n_seq, home_rows, feat_mp), "seq")
    x_home = jnp.sum(got.astype(jnp.float32), axis=0)

    square_sum = jnp.sum(gather_by_exchange(jnp.sum(x_home * x_home, axis=-1), "mp", n_mp), axis=0)
    normed = (x_home * lax.rsqrt(square_sum[:, None] / D + EPS) * attn_gain).astype(jnp.bfloat16)
    normed_all = gather_by_exchange(normed, "seq", n_seq).reshape(total_rows, feat_mp)

    qkv_part = jnp.dot(normed_all, w_qkv, preferred_element_type=jnp.float32)
    attn_rows = total_rows // n_mp
    qkv_got = exchange(qkv_part.reshape(n_mp, attn_rows, qkv_part.shape[-1]), "mp")
    qkv_cols = jnp.sum(qkv_got, axis=0).astype(jnp.bfloat16)
    qkv_rows = gather_by_exchange(qkv_cols, "seq", n_seq).transpose(1, 0, 2).reshape(attn_rows, -1)

    request_count = group_ids.shape[0]
    groups_per = QUERY_HEADS // KEY_VALUE_HEADS
    qf = QUERY_HEADS * HEAD_SIZE
    kf = KEY_VALUE_HEADS * HEAD_SIZE
    q = qkv_rows[:, :qf].reshape(request_count, NEW_TOKENS, KEY_VALUE_HEADS, groups_per, HEAD_SIZE)
    k_new = qkv_rows[:, qf : qf + kf].reshape(request_count, NEW_TOKENS, KEY_VALUE_HEADS, HEAD_SIZE)
    v_new = qkv_rows[:, qf + kf :].reshape(request_count, NEW_TOKENS, KEY_VALUE_HEADS, HEAD_SIZE)

    pre_rows = prompt_cache.shape[2]
    suf_rows = request_cache.shape[2]
    first_group = (group_ids == 0)[:, None, None]
    pre_k = jnp.where(first_group, prompt_cache[0, 0][None], prompt_cache[0, 1][None])
    pre_v = jnp.where(first_group, prompt_cache[1, 0][None], prompt_cache[1, 1][None])
    keys = jnp.concatenate([pre_k, request_cache[0]], axis=1).reshape(
        request_count, pre_rows + suf_rows, KEY_VALUE_HEADS, HEAD_SIZE
    )
    values = jnp.concatenate([pre_v, request_cache[1]], axis=1).reshape(
        request_count, pre_rows + suf_rows, KEY_VALUE_HEADS, HEAD_SIZE
    )
    own_prefix = jnp.where(group_ids == 0, prefix_len[0], prefix_len[1])
    pre_pos = s * pre_rows + jnp.arange(pre_rows, dtype=jnp.int32)
    suf_pos = s * suf_rows + jnp.arange(suf_rows, dtype=jnp.int32)
    valid = jnp.concatenate(
        [pre_pos[None, :] < own_prefix[:, None], suf_pos[None, :] < suffix_len[:, None]], axis=1
    )[:, None, None, None, :]
    score_scale = 1.0 / math.sqrt(HEAD_SIZE)
    scores = jnp.einsum("jtkgd,jpkd->jtkgp", q, keys, preferred_element_type=jnp.float32) * score_scale
    scores = jnp.where(valid, scores, NEG)
    block_max = jnp.max(scores, axis=-1)
    probs = jnp.where(valid, jnp.exp(scores - block_max[..., None]), 0.0)
    block_sum = jnp.sum(probs, axis=-1)
    block_acc = jnp.einsum(
        "jtkgp,jpkd->jtkgd", probs.astype(jnp.bfloat16), values, preferred_element_type=jnp.float32
    )

    new_scores = jnp.einsum("jtkgd,jukd->jtkgu", q, k_new, preferred_element_type=jnp.float32) * score_scale
    causal = (jnp.arange(NEW_TOKENS)[:, None] >= jnp.arange(NEW_TOKENS)[None, :])[None, :, None, None, :]
    new_scores = jnp.where(causal, new_scores, NEG)
    new_max = jnp.max(new_scores, axis=-1)
    new_probs = jnp.where(causal, jnp.exp(new_scores - new_max[..., None]), 0.0)
    new_sum = jnp.sum(new_probs, axis=-1)
    new_acc = jnp.einsum(
        "jtkgu,jukd->jtkgd", new_probs.astype(jnp.bfloat16), v_new, preferred_element_type=jnp.float32
    )

    fs = qf // n_seq
    acc_flat = block_acc.reshape(attn_rows, qf)
    acc_parts = acc_flat.reshape(attn_rows, n_seq, fs).transpose(1, 0, 2)
    head_pick = np.array([[(i * fs) // HEAD_SIZE, (i * fs + fs - 1) // HEAD_SIZE] for i in range(n_seq)])
    max_flat = block_max.reshape(attn_rows, QUERY_HEADS)
    sum_flat = block_sum.reshape(attn_rows, QUERY_HEADS)
    max_parts = max_flat[:, head_pick].transpose(1, 0, 2)
    sum_parts = sum_flat[:, head_pick].transpose(1, 0, 2)
    merged = exchange(jnp.concatenate([acc_parts, max_parts, sum_parts], axis=-1), "seq")
    got_acc = merged[..., :fs]
    feat_ids = s * fs + jnp.arange(fs, dtype=jnp.int32)
    second = (feat_ids // HEAD_SIZE - (s * fs) // HEAD_SIZE) == 1
    got_max = jnp.where(second, merged[..., fs + 1 : fs + 2], merged[..., fs : fs + 1])
    got_sum = jnp.where(second, merged[..., fs + 3 : fs + 4], merged[..., fs + 2 : fs + 3])
    own_heads = feat_ids // HEAD_SIZE
    n_max = jnp.take(new_max.reshape(attn_rows, QUERY_HEADS), own_heads, axis=1)
    n_sum = jnp.take(new_sum.reshape(attn_rows, QUERY_HEADS), own_heads, axis=1)
    n_acc = lax.dynamic_slice_in_dim(new_acc.reshape(attn_rows, qf), s * fs, fs, 1)
    overall = jnp.maximum(jnp.max(got_max, axis=0), n_max)
    cache_weight = jnp.exp(got_max - overall)
    own_weight = jnp.exp(n_max - overall)
    denominator = jnp.sum(cache_weight * got_sum, axis=0) + own_weight * n_sum
    numerator = jnp.sum(cache_weight * got_acc, axis=0) + own_weight * n_acc
    attended = (numerator / denominator).astype(jnp.bfloat16)

    att_all = gather_by_exchange(attended, "mp", n_mp).reshape(total_rows, fs)
    out_part = jnp.dot(att_all, w_out, preferred_element_type=jnp.float32)
    out_got = exchange(out_part.reshape(n_seq, home_rows, out_part.shape[-1]), "seq")
    x2 = (x_home + jnp.sum(out_got, axis=0)).astype(jnp.bfloat16)

    route_blocks = routes.reshape(n_seq, home_rows, TOPK)
    experts_all = jnp.arange(E, dtype=jnp.int32)
    hit = jnp.any(route_blocks[:, :, :, None] == experts_all, axis=2)
    hit_count = hit.astype(jnp.int32)
    ahead = jnp.cumsum(hit_count, axis=1) - hit_count
    chosen = hit[..., None] & (ahead[..., None] == jnp.arange(MOST, dtype=jnp.int32))
    chosen = jnp.transpose(chosen, (0, 2, 3, 1)).astype(jnp.bfloat16)
    member = hit.astype(jnp.bfloat16)

    home_table = chosen[s]
    x2_full = gather_by_exchange(x2, "mp", n_mp).transpose(1, 0, 2).reshape(home_rows, D)
    floats2 = x2_full.astype(jnp.float32)
    mean_sq = jnp.mean(floats2 * floats2, axis=-1, keepdims=True)
    normed2 = (floats2 * lax.rsqrt(mean_sq + EPS) * moe_gain).astype(jnp.bfloat16)
    dispatch = jnp.einsum("esr,rf->esf", home_table, normed2, preferred_element_type=jnp.float32).astype(
        jnp.bfloat16
    )
    slot_normed = exchange(dispatch, "seq").reshape(n_seq * MOST, D)

    expert = s
    expert_table = chosen[:, expert]
    slot_member = jnp.einsum(
        "bsr,bre->bse", expert_table, member, preferred_element_type=jnp.float32
    ).reshape(n_seq * MOST, E)
    logits = jnp.dot(slot_normed, w_router, preferred_element_type=jnp.float32)
    which = (experts_all == expert).astype(jnp.float32)
    own_flag = jnp.sum(slot_member * which, axis=1)
    own_logit = jnp.sum(logits * which, axis=1)
    denom = jnp.sum(jnp.where(slot_member > 0, jnp.exp(logits), 0.0), axis=1)
    share = own_flag * jnp.exp(own_logit) / (denom + 1.0 - own_flag)

    gate_up = w_gate_up[0]
    half = gate_up.shape[1]
    both = lax.dot_general(
        slot_normed,
        gate_up.reshape(2 * half, D),
        (((1,), (1,)), ((), ())),
        preferred_element_type=jnp.float32,
    )
    hidden = (jnp.maximum(both[:, :half], 0.0) * both[:, half:]).astype(jnp.bfloat16)
    hidden_all = gather_by_exchange(hidden, "mp", n_mp)
    hidden_all = hidden_all.transpose(1, 0, 2).reshape(n_seq * MOST, n_mp * half)
    down_cols = exchange(w_down[0].reshape(half, n_mp, feat_mp).transpose(1, 0, 2), "mp")
    down_cols = down_cols.reshape(n_mp * half, feat_mp)
    expert_out = jnp.dot(hidden_all, down_cols, preferred_element_type=jnp.float32).astype(jnp.bfloat16)
    weighted = (share[:, None] * expert_out.astype(jnp.float32)).astype(jnp.bfloat16)
    back = exchange(weighted.reshape(n_seq, MOST, feat_mp), "seq")
    terms = jnp.einsum("esr,esf->rf", home_table, back, preferred_element_type=jnp.float32)
    final = (x2.astype(jnp.float32) + terms).astype(jnp.bfloat16)
    return final.reshape(home_rows // NEW_TOKENS, NEW_TOKENS, feat_mp)


def solution(mesh):
    in_specs = (
        P(),
        P("seq", "mp"),
        P("mp"),
        P("mp", "seq"),
        P("seq", "mp"),
        P(None, "mp", "seq", None),
        P(None, "mp", "seq", None),
        P("mp"),
        P("mp"),
        P("mp"),
        P(),
        P(),
        P("seq", None, "mp", None),
        P("seq", "mp", None),
        P(),
    )
    out_specs = P("seq", None, "mp")
    return jax.shard_map(
        on_device, mesh=mesh, in_specs=in_specs, out_specs=out_specs, check_vma=False
    )
```

```python
import math

import numpy as np

import jax
import jax.numpy as jnp
from jax import lax
from jax.sharding import PartitionSpec as P

D = 1536
QUERY_HEADS = 12
KEY_VALUE_HEADS = 2
HEAD_SIZE = 128
E = 32
TOPK = 4
NEW_TOKENS = 4
MOST = 8

EPS = 1e-06
NEG = -1e30


def exchange(values, axis):
    return lax.all_to_all(values, axis, 0, 0, tiled=True)


def gather_by_exchange(values, axis, n):
    return lax.all_to_all(jnp.broadcast_to(values[None], (n,) + values.shape), axis, 0, 0, tiled=True)


def on_device(
    token_ids,
    embedding,
    attn_gain,
    w_qkv,
    w_out,
    prompt_cache,
    request_cache,
    group_ids,
    prefix_len,
    suffix_len,
    moe_gain,
    w_router,
    w_gate_up,
    w_down,
    routes,
):
    n_seq = lax.axis_size("seq")
    n_mp = lax.axis_size("mp")
    s = lax.axis_index("seq")
    total_rows = token_ids.shape[0] * NEW_TOKENS
    home_rows = total_rows // n_seq
    feat_mp = embedding.shape[1]

    vocab_rows = embedding.shape[0]
    local_ids = token_ids.reshape(total_rows) - s * vocab_rows
    inside = (local_ids >= 0) & (local_ids < vocab_rows)
    looked = jnp.take(embedding, jnp.clip(local_ids, 0, vocab_rows - 1), axis=0)
    looked = jnp.where(inside[:, None], looked, jnp.zeros_like(looked))
    got = exchange(looked.reshape(n_seq, home_rows, feat_mp), "seq")
    x_home = jnp.sum(got.astype(jnp.float32), axis=0)

    half = w_down.shape[1]
    down_send = w_down[0].reshape(half, n_mp, feat_mp).transpose(1, 0, 2).reshape(n_mp, half * feat_mp)
    own_squares = jnp.broadcast_to(jnp.sum(x_home * x_home, axis=-1)[None], (n_mp, home_rows))
    mp_got = exchange(jnp.concatenate([own_squares, down_send.astype(jnp.float32)], axis=1), "mp")
    square_sum = jnp.sum(mp_got[:, :home_rows], axis=0)
    down_cols = mp_got[:, home_rows:].astype(jnp.bfloat16).reshape(n_mp * half, feat_mp)
    normed = (x_home * lax.rsqrt(square_sum[:, None] / D + EPS) * attn_gain).astype(jnp.bfloat16)
    normed_all = gather_by_exchange(normed, "seq", n_seq).reshape(total_rows, feat_mp)

    qkv_part = jnp.dot(normed_all, w_qkv, preferred_element_type=jnp.float32)
    attn_rows = total_rows // n_mp
    qkv_got = exchange(qkv_part.reshape(n_mp, attn_rows, qkv_part.shape[-1]), "mp")
    qkv_cols = jnp.sum(qkv_got, axis=0).astype(jnp.bfloat16)
    qkv_rows = gather_by_exchange(qkv_cols, "seq", n_seq).transpose(1, 0, 2).reshape(attn_rows, -1)

    request_count = group_ids.shape[0]
    groups_per = QUERY_HEADS // KEY_VALUE_HEADS
    qf = QUERY_HEADS * HEAD_SIZE
    kf = KEY_VALUE_HEADS * HEAD_SIZE
    q = qkv_rows[:, :qf].reshape(request_count, NEW_TOKENS, KEY_VALUE_HEADS, groups_per, HEAD_SIZE)
    k_new = qkv_rows[:, qf : qf + kf].reshape(request_count, NEW_TOKENS, KEY_VALUE_HEADS, HEAD_SIZE)
    v_new = qkv_rows[:, qf + kf :].reshape(request_count, NEW_TOKENS, KEY_VALUE_HEADS, HEAD_SIZE)

    pre_rows = prompt_cache.shape[2]
    suf_rows = request_cache.shape[2]
    first_group = (group_ids == 0)[:, None, None]
    pre_k = jnp.where(first_group, prompt_cache[0, 0][None], prompt_cache[0, 1][None])
    pre_v = jnp.where(first_group, prompt_cache[1, 0][None], prompt_cache[1, 1][None])
    keys = jnp.concatenate([pre_k, request_cache[0]], axis=1).reshape(
        request_count, pre_rows + suf_rows, KEY_VALUE_HEADS, HEAD_SIZE
    )
    values = jnp.concatenate([pre_v, request_cache[1]], axis=1).reshape(
        request_count, pre_rows + suf_rows, KEY_VALUE_HEADS, HEAD_SIZE
    )
    own_prefix = jnp.where(group_ids == 0, prefix_len[0], prefix_len[1])
    pre_pos = s * pre_rows + jnp.arange(pre_rows, dtype=jnp.int32)
    suf_pos = s * suf_rows + jnp.arange(suf_rows, dtype=jnp.int32)
    valid = jnp.concatenate(
        [pre_pos[None, :] < own_prefix[:, None], suf_pos[None, :] < suffix_len[:, None]], axis=1
    )[:, None, None, None, :]
    score_scale = 1.0 / math.sqrt(HEAD_SIZE)
    scores = jnp.einsum("jtkgd,jpkd->jtkgp", q, keys, preferred_element_type=jnp.float32) * score_scale
    scores = jnp.where(valid, scores, NEG)
    block_max = jnp.max(scores, axis=-1)
    probs = jnp.where(valid, jnp.exp(scores - block_max[..., None]), 0.0)
    block_sum = jnp.sum(probs, axis=-1)
    block_acc = jnp.einsum(
        "jtkgp,jpkd->jtkgd", probs.astype(jnp.bfloat16), values, preferred_element_type=jnp.float32
    )

    new_scores = jnp.einsum("jtkgd,jukd->jtkgu", q, k_new, preferred_element_type=jnp.float32) * score_scale
    causal = (jnp.arange(NEW_TOKENS)[:, None] >= jnp.arange(NEW_TOKENS)[None, :])[None, :, None, None, :]
    new_scores = jnp.where(causal, new_scores, NEG)
    new_max = jnp.max(new_scores, axis=-1)
    new_probs = jnp.where(causal, jnp.exp(new_scores - new_max[..., None]), 0.0)
    new_sum = jnp.sum(new_probs, axis=-1)
    new_acc = jnp.einsum(
        "jtkgu,jukd->jtkgd", new_probs.astype(jnp.bfloat16), v_new, preferred_element_type=jnp.float32
    )

    fs = qf // n_seq
    acc_flat = block_acc.reshape(attn_rows, qf)
    acc_parts = acc_flat.reshape(attn_rows, n_seq, fs).transpose(1, 0, 2)
    head_pick = np.array([[(i * fs) // HEAD_SIZE, (i * fs + fs - 1) // HEAD_SIZE] for i in range(n_seq)])
    max_flat = block_max.reshape(attn_rows, QUERY_HEADS)
    sum_flat = block_sum.reshape(attn_rows, QUERY_HEADS)
    max_parts = max_flat[:, head_pick].transpose(1, 0, 2)
    sum_parts = sum_flat[:, head_pick].transpose(1, 0, 2)
    merged = exchange(jnp.concatenate([acc_parts, max_parts, sum_parts], axis=-1), "seq")
    got_acc = merged[..., :fs]
    feat_ids = s * fs + jnp.arange(fs, dtype=jnp.int32)
    second = (feat_ids // HEAD_SIZE - (s * fs) // HEAD_SIZE) == 1
    got_max = jnp.where(second, merged[..., fs + 1 : fs + 2], merged[..., fs : fs + 1])
    got_sum = jnp.where(second, merged[..., fs + 3 : fs + 4], merged[..., fs + 2 : fs + 3])
    own_heads = feat_ids // HEAD_SIZE
    n_max = jnp.take(new_max.reshape(attn_rows, QUERY_HEADS), own_heads, axis=1)
    n_sum = jnp.take(new_sum.reshape(attn_rows, QUERY_HEADS), own_heads, axis=1)
    n_acc = lax.dynamic_slice_in_dim(new_acc.reshape(attn_rows, qf), s * fs, fs, 1)
    overall = jnp.maximum(jnp.max(got_max, axis=0), n_max)
    cache_weight = jnp.exp(got_max - overall)
    own_weight = jnp.exp(n_max - overall)
    denominator = jnp.sum(cache_weight * got_sum, axis=0) + own_weight * n_sum
    numerator = jnp.sum(cache_weight * got_acc, axis=0) + own_weight * n_acc
    attended = (numerator / denominator).astype(jnp.bfloat16)

    att_all = gather_by_exchange(attended, "mp", n_mp).reshape(total_rows, fs)
    out_part = jnp.dot(att_all, w_out, preferred_element_type=jnp.float32)
    out_got = exchange(out_part.reshape(n_seq, home_rows, out_part.shape[-1]), "seq")
    x2 = (x_home + jnp.sum(out_got, axis=0)).astype(jnp.bfloat16)

    route_blocks = routes.reshape(n_seq, home_rows, TOPK)
    experts_all = jnp.arange(E, dtype=jnp.int32)
    hit = jnp.any(route_blocks[:, :, :, None] == experts_all, axis=2)
    hit_count = hit.astype(jnp.int32)
    ahead = jnp.cumsum(hit_count, axis=1) - hit_count
    chosen = hit[..., None] & (ahead[..., None] == jnp.arange(MOST, dtype=jnp.int32))
    chosen = jnp.transpose(chosen, (0, 2, 3, 1)).astype(jnp.bfloat16)
    member = hit.astype(jnp.bfloat16)

    home_table = chosen[s]
    x2_full = gather_by_exchange(x2, "mp", n_mp).transpose(1, 0, 2).reshape(home_rows, D)
    floats2 = x2_full.astype(jnp.float32)
    mean_sq = jnp.mean(floats2 * floats2, axis=-1, keepdims=True)
    normed2 = (floats2 * lax.rsqrt(mean_sq + EPS) * moe_gain).astype(jnp.bfloat16)
    dispatch = jnp.einsum("esr,rf->esf", home_table, normed2, preferred_element_type=jnp.float32).astype(
        jnp.bfloat16
    )
    slot_normed = exchange(dispatch, "seq").reshape(n_seq * MOST, D)

    expert = s
    expert_table = chosen[:, expert]
    slot_member = jnp.einsum(
        "bsr,bre->bse", expert_table, member, preferred_element_type=jnp.float32
    ).reshape(n_seq * MOST, E)
    logits = jnp.dot(slot_normed, w_router, preferred_element_type=jnp.float32)
    which = (experts_all == expert).astype(jnp.float32)
    own_flag = jnp.sum(slot_member * which, axis=1)
    own_logit = jnp.sum(logits * which, axis=1)
    denom = jnp.sum(jnp.where(slot_member > 0, jnp.exp(logits), 0.0), axis=1)
    share = own_flag * jnp.exp(own_logit) / (denom + 1.0 - own_flag)

    gate_up = w_gate_up[0]
    half = gate_up.shape[1]
    both = lax.dot_general(
        slot_normed,
        gate_up.reshape(2 * half, D),
        (((1,), (1,)), ((), ())),
        preferred_element_type=jnp.float32,
    )
    hidden = (jnp.maximum(both[:, :half], 0.0) * both[:, half:]).astype(jnp.bfloat16)
    hidden_all = gather_by_exchange(hidden, "mp", n_mp)
    hidden_all = hidden_all.transpose(1, 0, 2).reshape(n_seq * MOST, n_mp * half)
    expert_out = jnp.dot(hidden_all, down_cols, preferred_element_type=jnp.float32).astype(jnp.bfloat16)
    weighted = (share[:, None] * expert_out.astype(jnp.float32)).astype(jnp.bfloat16)
    back = exchange(weighted.reshape(n_seq, MOST, feat_mp), "seq")
    terms = jnp.einsum("esr,esf->rf", home_table, back, preferred_element_type=jnp.float32)
    final = (x2.astype(jnp.float32) + terms).astype(jnp.bfloat16)
    return final.reshape(home_rows // NEW_TOKENS, NEW_TOKENS, feat_mp)


def solution(mesh):
    in_specs = (
        P(),
        P("seq", "mp"),
        P("mp"),
        P("mp", "seq"),
        P("seq", "mp"),
        P(None, "mp", "seq", None),
        P(None, "mp", "seq", None),
        P("mp"),
        P("mp"),
        P("mp"),
        P(),
        P(),
        P("seq", None, "mp", None),
        P("seq", "mp", None),
        P(),
    )
    out_specs = P("seq", None, "mp")
    return jax.shard_map(
        on_device, mesh=mesh, in_specs=in_specs, out_specs=out_specs, check_vma=False
    )
```
